512 devices in a mesh: section: 32 (over y, x), ctx: 16 (over z, core).
Axes of the slice: x: 4, y: 8, z: 8, core: 2. Of those that a mesh axis runs over, the one named last changes fastest.
Arguments:
- queries: bfloat16 [32, 2048, 2048], P('section', 'ctx'), may hold values from -6 to 6
- key_states: bfloat16 [32, 2048, 2048], P('section', 'ctx'), may hold values from -6 to 6
- value_states: bfloat16 [32, 2048, 2048], P('section', 'ctx'), may hold values from -6 to 6
- upstream: bfloat16 [32, 2048, 2048], P('section', 'ctx'), may hold values from -6 to 6
- layout: int32 [32, 16, 16, 4], P('section', 'ctx'), may hold values from 0 to 15, as said below
- segments: int32 [32, 16], P('section'), may hold values from 0 to 4, never falling along the last dimension, each value on 1 to 8 neighbouring positions
Outputs:
- attended: bfloat16 [32, 2048, 2048], P('section', 'ctx')
- grad_queries: bfloat16 [32, 2048, 2048], P('section', 'ctx')
- grad_keys: bfloat16 [32, 2048, 2048], P('section', 'ctx')
- grad_values: bfloat16 [32, 2048, 2048], P('section', 'ctx')
The draws below stay inside these ranges and needn't reach their ends.
Inputs may be any that keep to these rules, and one draw needn't show every extreme that they name: `layout`: for section s, head h and query block a the four entries are a, a - 1, a - 2 and a - 3 - r for some r from 0 to 12, each taken modulo 16; they are distinct.
All inputs are finite; a program needn't handle non-finite values.
Results may differ from the reference program's by a relative error of at most 0.04.
Values may be sent and summed in bfloat16 or wider, within the bound.
No kernel may reach another device: no remote copies, remote signals or barrier semaphores. Data moves between devices by JAX's collectives and lax.ppermute only.
A program may use at most 64 MiB of HBM per device.

```python
import math
import jax
import jax.numpy as jnp
import numpy as np
from jax import lax

HEADS = 16
DH = 128
BLK = 128
TOKENS = 2048
NB = 16
SECTIONS = 32


def base_field(key, salt):
    field_key = jax.random.fold_in(key, salt)
    field_shape = (SECTIONS, NB, BLK, HEADS * DH)
    field = jnp.clip(jax.random.normal(field_key, field_shape, jnp.float32), -6.0, 6.0)
    return field


def draw_queries(key, part):
    field = base_field(key, 1)
    return field.reshape(SECTIONS, NB * BLK, HEADS * DH).astype(jnp.bfloat16)


def draw_key_states(key, part):
    field = base_field(key, 2)
    return field.reshape(SECTIONS, NB * BLK, HEADS * DH).astype(jnp.bfloat16)


def draw_layout(key, part):
    stride = jax.random.randint(jax.random.fold_in(key, 7), (SECTIONS, HEADS, NB, 1), 0, NB - 3)
    current = jnp.broadcast_to(jnp.arange(NB).reshape(1, 1, NB, 1), stride.shape)
    slot_blocks = jnp.concatenate([current, current - 1, current - 2, current - 3 - stride], axis=3)
    return jnp.mod(slot_blocks, NB).astype(jnp.int32)


def steps_of(key, extent, cuts, low, largest):
    level = 1.0
    for dim, shards_of in cuts:
        steps = jax.random.uniform(jax.random.fold_in(jax.random.fold_in(key, 6), dim), (shards_of,), jnp.float32, low / len(cuts), largest / len(cuts))
        level = level * jnp.repeat(jnp.exp(steps), extent[dim] // shards_of).reshape((-1,) + (1,) * (len(extent) - 1 - dim))
    return level


def length_profile(count, total, reach, skew):
    portions = [(1 << 20) // math.isqrt(rank ** skew) + 1 for rank in range(2, count + 1)]
    rest, counts = total - reach - (count - 1), [1] * (count - 1)
    while rest > 0:
        movable = [i for i in range(count - 1) if counts[i] < reach]
        whole, remaining = sum([portions[i] for i in movable]), rest
        for i in movable:
            extra = min(reach - counts[i], max(1, remaining * portions[i] // whole), rest)
            counts[i] = counts[i] + extra
            rest = rest - extra
    return np.array([reach] + counts)


def uneven(stream_key, count, total, reach, slope):
    if count == 2:
        one = jax.random.randint(stream_key, (), max(1, total - reach), min(reach, total - 1) + 1)
        return jnp.stack([one, total - one])
    tallies = jnp.asarray(length_profile(count, total, reach, slope), jnp.int32)
    couples = (count - 1) // 2
    source_of, receiver = tallies[1:1 + 2 * couples:2], tallies[2:2 + 2 * couples:2]
    room = jnp.minimum(source_of - 1, reach - receiver)
    passed = jax.random.randint(jax.random.fold_in(stream_key, 1), (couples,), 0, 1 << 20) % (room + 1)
    tallies = tallies.at[1:1 + 2 * couples:2].set(source_of - passed).at[2:2 + 2 * couples:2].set(receiver + passed)
    return tallies[jax.random.permutation(jax.random.fold_in(stream_key, 2), count)]


def noise(own_key, dims, width, most, shards=(), kind=jnp.bfloat16):
    values = width * jax.random.normal(own_key, dims, jnp.float32)
    if shards:
        values = values * steps_of(own_key, dims, shards, -0.22, 0.18)
    return jnp.clip(values, -most, most).astype(kind)


def setup_inputs(seed: int = 0) -> dict:
    keys = jax.random.split(jax.random.key(seed), 7)
    return {
        "queries": draw_queries(jax.random.fold_in(keys[6], 71), 0),
        "key_states": draw_key_states(jax.random.fold_in(keys[6], 71), 0),
        "value_states": noise(keys[2], (SECTIONS, TOKENS, HEADS * DH), 1.0, 6.0, ((0, 32), (1, 16))),
        "upstream": noise(keys[3], (SECTIONS, TOKENS, HEADS * DH), 1.0, 6.0, ((0, 32), (1, 16))),
        "layout": draw_layout(jax.random.fold_in(keys[6], 71), 0),
        "segments": jax.vmap(lambda own: jnp.searchsorted(jnp.cumsum(uneven(own, NB // 4 + 1, NB, NB // 2, 0)), jnp.arange(NB), side="right"))(jax.random.split(keys[5], SECTIONS)).reshape((SECTIONS, NB)).astype(jnp.int32),
    }


def gather_blocks(blocks, layout):
    head_index = jnp.arange(layout.shape[0])[:, None, None]
    picked = blocks[layout, :, head_index, :]
    return picked.reshape(layout.shape[0], layout.shape[1], layout.shape[2] * blocks.shape[1], blocks.shape[3])

def visible_mask(layout, segments, block_rows):
    block_count = layout.shape[1]
    query_block = jnp.arange(block_count)[None, :, None]
    same_doc = segments[layout] == segments[query_block]
    earlier = layout < query_block
    position = jnp.arange(block_rows)
    within = position[None, None, None, None, :] <= position[None, None, :, None, None]
    diagonal = (layout == query_block)[:, :, None, :, None] & within
    visible = same_doc[:, :, None, :, None] & (earlier[:, :, None, :, None] | diagonal)
    return visible.reshape(layout.shape[0], block_count, block_rows, layout.shape[2] * block_rows)

def scatter_blocks(picked, layout, block_rows):
    head_count, block_count, slot_count = layout.shape
    head_dim = picked.shape[-1]
    pieces = picked.reshape(head_count, block_count, slot_count, block_rows * head_dim)
    onehot = (layout[..., None] == jnp.arange(block_count)).astype(jnp.float32)
    summed = jnp.einsum('hasb,hase->hbe', onehot, pieces, precision=lax.Precision.HIGHEST)
    return summed.reshape(head_count, block_count, block_rows, head_dim).transpose(1, 2, 0, 3)

def section_pass(inputs):
    queries, key_states, value_states, grad_out, layout, segments = inputs
    block_shape = (NB, BLK, HEADS, DH)
    score_scale = 1.0 / math.sqrt(DH)
    query_blocks = queries.reshape(block_shape).astype(jnp.float32)
    key_rows = gather_blocks(key_states.reshape(block_shape), layout).astype(jnp.float32)
    value_rows = gather_blocks(value_states.reshape(block_shape), layout).astype(jnp.float32)
    visible = visible_mask(layout, segments, BLK)
    scores = jnp.einsum('aihd,hamd->haim', query_blocks, key_rows) * score_scale
    scores = jnp.where(visible, scores, -jnp.inf)
    row_max = lax.optimization_barrier(jnp.max(scores, axis=-1, keepdims=True))
    raised = jnp.exp(scores - row_max)
    weights = raised / lax.optimization_barrier(jnp.sum(raised, axis=-1, keepdims=True))
    weights_low = lax.optimization_barrier(weights.astype(jnp.bfloat16)).astype(jnp.float32)
    attended = jnp.einsum('haim,hamd->aihd', weights_low, value_rows).astype(jnp.bfloat16)
    attended_wide = lax.optimization_barrier(attended).astype(jnp.float32)
    grad_blocks = grad_out.reshape(block_shape).astype(jnp.float32)
    grad_weight = jnp.einsum('aihd,hamd->haim', grad_blocks, value_rows)
    row_inner = lax.optimization_barrier(jnp.sum(grad_blocks * attended_wide, axis=-1)).transpose(2, 0, 1)[..., None]
    grad_score = (weights * (grad_weight - row_inner)).astype(jnp.bfloat16)
    grad_score = lax.optimization_barrier(grad_score).astype(jnp.float32)
    grad_query = (jnp.einsum('haim,hamd->aihd', grad_score, key_rows) * score_scale).astype(jnp.bfloat16)
    grad_key_rows = jnp.einsum('haim,aihd->hamd', grad_score, query_blocks) * score_scale
    grad_value_rows = jnp.einsum('haim,aihd->hamd', weights_low, grad_blocks)
    grad_key = scatter_blocks(grad_key_rows, layout, BLK).astype(jnp.bfloat16)
    grad_value = scatter_blocks(grad_value_rows, layout, BLK).astype(jnp.bfloat16)
    flat_shape = (TOKENS, HEADS * DH)
    return (attended.reshape(flat_shape), grad_query.reshape(flat_shape), grad_key.reshape(flat_shape), grad_value.reshape(flat_shape))

def reference(queries, key_states, value_states, upstream, layout, segments):
    grad_all = jnp.roll(upstream, -1, axis=0)
    results = lax.map(section_pass, (queries, key_states, value_states, grad_all, layout, segments))
    return (results[0], results[1], results[2], results[3])
```

```python
import functools
import math

import jax
import jax.numpy as jnp
from jax import lax
from jax.experimental import pallas as pl
from jax.experimental.pallas import tpu as pltpu
from jax.sharding import PartitionSpec as P

HEADS = 16
BLK = 128
SLOTS = 4


def passed_along(value, axis, steps):
    count = lax.axis_size(axis)
    pairs = [(source, (source + steps) % count) for source in range(count)]
    return lax.ppermute(value, axis, pairs)


def head_kernel(lay_ref, seg_ref, qkv_ref, grad_ref, out_ref, dk_acc, dv_acc):
    block_count = qkv_ref.shape[0]
    head_dim = qkv_ref.shape[-1]
    score_scale = 1.0 / math.sqrt(head_dim)
    dk_acc[...] = jnp.zeros_like(dk_acc)
    dv_acc[...] = jnp.zeros_like(dv_acc)
    row = lax.broadcasted_iota(jnp.int32, (BLK, BLK), 0)
    col = lax.broadcasted_iota(jnp.int32, (BLK, BLK), 1)

    def body(a, carry):
        q = qkv_ref[a, 0]
        g = grad_ref[a]
        seg_a = seg_ref[a]
        blocks = [lay_ref[a * SLOTS + j] for j in range(SLOTS)]
        key_rows = jnp.concatenate([qkv_ref[b, 1] for b in blocks], axis=0)
        value_rows = jnp.concatenate([qkv_ref[b, 2] for b in blocks], axis=0)
        masks = []
        for b in blocks:
            diag = (b == a).astype(jnp.int32)
            open_ = jnp.logical_and(b < a, seg_ref[b] == seg_a).astype(jnp.int32)
            limit = row * diag + (1 - diag) * (open_ * BLK - 1)
            masks.append(col <= limit)
        visible = jnp.concatenate(masks, axis=1)
        scores = lax.dot_general(
            q, key_rows, (((1,), (1,)), ((), ())), preferred_element_type=jnp.float32
        ) * score_scale
        scores = jnp.where(visible, scores, -jnp.inf)
        row_max = jnp.max(scores, axis=-1, keepdims=True)
        raised = jnp.exp(scores - row_max)
        weights = raised / jnp.sum(raised, axis=-1, keepdims=True)
        weights_low = weights.astype(jnp.bfloat16)
        attended = jnp.dot(
            weights_low, value_rows, preferred_element_type=jnp.float32
        ).astype(jnp.bfloat16)
        grad_weight = lax.dot_general(
            g, value_rows, (((1,), (1,)), ((), ())), preferred_element_type=jnp.float32
        )
        row_inner = jnp.sum(
            g.astype(jnp.float32) * attended.astype(jnp.float32), axis=-1, keepdims=True
        )
        grad_score = (weights * (grad_weight - row_inner)).astype(jnp.bfloat16)
        grad_query = jnp.dot(grad_score, key_rows, preferred_element_type=jnp.float32)
        out_ref[a, 0] = attended
        out_ref[a, 1] = (grad_query * score_scale).astype(jnp.bfloat16)
        grad_key_rows = lax.dot_general(
            grad_score, q, (((0,), (0,)), ((), ())), preferred_element_type=jnp.float32
        ) * score_scale
        grad_value_rows = lax.dot_general(
            weights_low, g, (((0,), (0,)), ((), ())), preferred_element_type=jnp.float32
        )
        for j, b in enumerate(blocks):
            dk_acc[b] += grad_key_rows[j * BLK:(j + 1) * BLK]
            dv_acc[b] += grad_value_rows[j * BLK:(j + 1) * BLK]
        return carry

    lax.fori_loop(0, block_count, body, 0)
    for b in range(block_count):
        out_ref[b, 2] = dk_acc[b].astype(jnp.bfloat16)
        out_ref[b, 3] = dv_acc[b].astype(jnp.bfloat16)


def head_pass(plan, documents, qkv, grad):
    block_count, _, rows, head_dim = qkv.shape
    flops = 6 * 2 * block_count * rows * SLOTS * rows * head_dim
    return pl.pallas_call(
        head_kernel,
        out_shape=jax.ShapeDtypeStruct((block_count, 4, rows, head_dim), jnp.bfloat16),
        in_specs=[
            pl.BlockSpec(memory_space=pltpu.SMEM),
            pl.BlockSpec(memory_space=pltpu.SMEM),
            pl.BlockSpec(memory_space=pltpu.VMEM),
            pl.BlockSpec(memory_space=pltpu.VMEM),
        ],
        out_specs=pl.BlockSpec(memory_space=pltpu.VMEM),
        scratch_shapes=[
            pltpu.VMEM((block_count, rows, head_dim), jnp.float32),
            pltpu.VMEM((block_count, rows, head_dim), jnp.float32),
        ],
        cost_estimate=pl.CostEstimate(
            flops=flops,
            transcendentals=block_count * rows * SLOTS * rows,
            bytes_accessed=2 * 8 * block_count * rows * head_dim,
        ),
    )(plan, documents, qkv, grad)


def local(queries, key_states, value_states, upstream, layout, segments):
    section_rows, tok_dev, feature_width = queries.shape
    head_dim = feature_width // HEADS

    def head_major(field):
        return field.reshape(tok_dev, HEADS, head_dim).transpose(1, 0, 2)

    arrived = passed_along(upstream, "section", -1)
    qkv = jnp.stack(
        [head_major(queries), head_major(key_states), head_major(value_states)], axis=1
    )
    qkv = lax.all_to_all(qkv, "ctx", 0, 0, tiled=True)
    grad = lax.all_to_all(head_major(arrived), "ctx", 0, 0, tiled=True)
    block_count = qkv.shape[0]
    plan = layout[0, 0].reshape(block_count * SLOTS)
    documents = segments[0]
    results = head_pass(plan, documents, qkv, grad)
    back = lax.all_to_all(results, "ctx", 0, 0, tiled=True)

    def merge_heads(i):
        return back[:, i].transpose(1, 0, 2).reshape(section_rows, tok_dev, feature_width)

    return tuple(merge_heads(i) for i in range(4))


def solution(mesh):
    placed = (
        P("section", "ctx", None),
        P("section", "ctx", None),
        P("section", "ctx", None),
        P("section", "ctx", None),
        P("section", "ctx", None, None),
        P("section", None),
    )
    return jax.shard_map(
        local,
        mesh=mesh,
        in_specs=placed,
        out_specs=(
            P("section", "ctx", None),
            P("section", "ctx", None),
            P("section", "ctx", None),
            P("section", "ctx", None),
        ),
        check_vma=False,
    )
```

```python
import math

import jax
import jax.numpy as jnp
from jax import lax
from jax.experimental import pallas as pl
from jax.experimental.pallas import tpu as pltpu
from jax.sharding import PartitionSpec as P


HEADS = 16
BLK = 128
SLOTS = 4


def passed_along(value, axis, steps):
    count = lax.axis_size(axis)
    pairs = [(source, (source + steps) % count) for source in range(count)]
    return lax.ppermute(value, axis, pairs)


def key_rows_of(qkv_ref, blocks, which):
    return jnp.concatenate([qkv_ref[b, which] for b in blocks], axis=0)


def forward_kernel(lay_ref, seg_ref, qkv_ref, o_ref, w_ref):
    block_count = qkv_ref.shape[0]
    head_dim = qkv_ref.shape[-1]
    score_scale = 1.0 / math.sqrt(head_dim)
    row = lax.broadcasted_iota(jnp.int32, (BLK, BLK), 0)
    col = lax.broadcasted_iota(jnp.int32, (BLK, BLK), 1)

    def body(a, carry):
        q = qkv_ref[a, 0]
        seg_a = seg_ref[a]
        blocks = [lay_ref[a * SLOTS + j] for j in range(SLOTS)]
        key_rows = key_rows_of(qkv_ref, blocks, 1)
        value_rows = key_rows_of(qkv_ref, blocks, 2)
        masks = []
        for b in blocks:
            diag = (b == a).astype(jnp.int32)
            open_ = jnp.logical_and(b < a, seg_ref[b] == seg_a).astype(jnp.int32)
            limit = row * diag + (1 - diag) * (open_ * BLK - 1)
            masks.append(col <= limit)
        visible = jnp.concatenate(masks, axis=1)
        scores = lax.dot_general(
            q, key_rows, (((1,), (1,)), ((), ())), preferred_element_type=jnp.float32
        ) * score_scale
        scores = jnp.where(visible, scores, -jnp.inf)
        row_max = jnp.max(scores, axis=-1, keepdims=True)
        raised = jnp.exp(scores - row_max)
        weights = raised / jnp.sum(raised, axis=-1, keepdims=True)
        w_ref[a] = weights
        o_ref[a] = jnp.dot(
            weights.astype(jnp.bfloat16), value_rows, preferred_element_type=jnp.float32
        ).astype(jnp.bfloat16)
        return carry

    lax.fori_loop(0, block_count, body, 0)


def backward_kernel(lay_ref, qkv_ref, g_ref, o_ref, w_ref, out_ref, dk_acc, dv_acc):
    block_count = qkv_ref.shape[0]
    head_dim = qkv_ref.shape[-1]
    score_scale = 1.0 / math.sqrt(head_dim)
    dk_acc[...] = jnp.zeros_like(dk_acc)
    dv_acc[...] = jnp.zeros_like(dv_acc)

    def body(a, carry):
        q = qkv_ref[a, 0]
        g = g_ref[a]
        blocks = [lay_ref[a * SLOTS + j] for j in range(SLOTS)]
        key_rows = key_rows_of(qkv_ref, blocks, 1)
        value_rows = key_rows_of(qkv_ref, blocks, 2)
        weights = w_ref[a]
        weights_low = weights.astype(jnp.bfloat16)
        grad_weight = lax.dot_general(
            g, value_rows, (((1,), (1,)), ((), ())), preferred_element_type=jnp.float32
        )
        row_inner = jnp.sum(
            g.astype(jnp.float32) * o_ref[a].astype(jnp.float32), axis=-1, keepdims=True
        )
        grad_score = (weights * (grad_weight - row_inner)).astype(jnp.bfloat16)
        grad_query = jnp.dot(grad_score, key_rows, preferred_element_type=jnp.float32)
        out_ref[a, 0] = (grad_query * score_scale).astype(jnp.bfloat16)
        grad_key_rows = lax.dot_general(
            grad_score, q, (((0,), (0,)), ((), ())), preferred_element_type=jnp.float32
        ) * score_scale
        grad_value_rows = lax.dot_general(
            weights_low, g, (((0,), (0,)), ((), ())), preferred_element_type=jnp.float32
        )
        for j, b in enumerate(blocks):
            dk_acc[b] += grad_key_rows[j * BLK:(j + 1) * BLK]
            dv_acc[b] += grad_value_rows[j * BLK:(j + 1) * BLK]
        return carry

    lax.fori_loop(0, block_count, body, 0)
    for b in range(block_count):
        out_ref[b, 1] = dk_acc[b].astype(jnp.bfloat16)
        out_ref[b, 2] = dv_acc[b].astype(jnp.bfloat16)


def forward_pass(plan, documents, qkv):
    block_count, _, rows, head_dim = qkv.shape
    flops = 2 * 2 * block_count * rows * SLOTS * rows * head_dim
    return pl.pallas_call(
        forward_kernel,
        out_shape=[
            jax.ShapeDtypeStruct((block_count, rows, head_dim), jnp.bfloat16),
            jax.ShapeDtypeStruct((block_count, rows, SLOTS * rows), jnp.float32),
        ],
        in_specs=[
            pl.BlockSpec(memory_space=pltpu.SMEM),
            pl.BlockSpec(memory_space=pltpu.SMEM),
            pl.BlockSpec(memory_space=pltpu.VMEM),
        ],
        out_specs=[pl.BlockSpec(memory_space=pltpu.VMEM)] * 2,
        cost_estimate=pl.CostEstimate(
            flops=flops,
            transcendentals=block_count * rows * SLOTS * rows,
            bytes_accessed=2 * 4 * block_count * rows * head_dim
            + 4 * block_count * rows * SLOTS * rows,
        ),
    )(plan, documents, qkv)


def backward_pass(plan, qkv, grad, attended, weights):
    block_count, _, rows, head_dim = qkv.shape
    flops = 4 * 2 * block_count * rows * SLOTS * rows * head_dim
    return pl.pallas_call(
        backward_kernel,
        out_shape=jax.ShapeDtypeStruct((block_count, 3, rows, head_dim), jnp.bfloat16),
        in_specs=[pl.BlockSpec(memory_space=pltpu.SMEM)]
        + [pl.BlockSpec(memory_space=pltpu.VMEM)] * 4,
        out_specs=pl.BlockSpec(memory_space=pltpu.VMEM),
        scratch_shapes=[
            pltpu.VMEM((block_count, rows, head_dim), jnp.float32),
            pltpu.VMEM((block_count, rows, head_dim), jnp.float32),
        ],
        cost_estimate=pl.CostEstimate(
            flops=flops,
            transcendentals=0,
            bytes_accessed=2 * 9 * block_count * rows * head_dim
            + 4 * block_count * rows * SLOTS * rows,
        ),
    )(plan, qkv, grad, attended, weights)


def unshuffle_kernel(first_ref, rest_ref, *out_refs):
    head_count, _, head_dim = first_ref.shape
    for i, out_ref in enumerate(out_refs):
        for h in range(head_count):
            piece = first_ref[h] if i == 0 else rest_ref[h, i - 1]
            out_ref[0, :, h * head_dim:(h + 1) * head_dim] = piece


def unshuffle(first, rest, section_rows):
    head_count, arrays, rows, head_dim = rest.shape
    field = jax.ShapeDtypeStruct((section_rows, rows, head_count * head_dim), rest.dtype)
    return pl.pallas_call(
        unshuffle_kernel,
        out_shape=[field] * (arrays + 1),
        in_specs=[pl.BlockSpec(memory_space=pltpu.VMEM)] * 2,
        out_specs=[pl.BlockSpec(memory_space=pltpu.VMEM)] * (arrays + 1),
        cost_estimate=pl.CostEstimate(
            flops=0,
            transcendentals=0,
            bytes_accessed=4 * (first.size + rest.size),
        ),
    )(first, rest)


def local(queries, key_states, value_states, upstream, layout, segments):
    section_rows, tok_dev, feature_width = queries.shape
    head_dim = feature_width // HEADS

    def head_major(field):
        return field.reshape(tok_dev, HEADS, head_dim).transpose(1, 0, 2)

    fields = jnp.stack(
        [head_major(f) for f in (queries, key_states, value_states, upstream)], axis=1
    )
    fields = lax.all_to_all(fields, "ctx", 0, 0, tiled=True)
    block_count = fields.shape[0]
    plan = layout[0, 0].reshape(block_count * SLOTS)
    documents = segments[0]
    grad = passed_along(fields[:, 3], "section", -1)
    attended, weights = forward_pass(plan, documents, fields)
    attended_back = lax.all_to_all(attended, "ctx", 0, 0, tiled=True)
    results = backward_pass(plan, fields, grad, attended, weights)
    back = lax.all_to_all(results, "ctx", 0, 0, tiled=True)
    return tuple(unshuffle(attended_back, back, section_rows))


def solution(mesh):
    placed = (
        P("section", "ctx", None),
        P("section", "ctx", None),
        P("section", "ctx", None),
        P("section", "ctx", None),
        P("section", "ctx", None, None),
        P("section", None),
    )
    return jax.shard_map(
        local,
        mesh=mesh,
        in_specs=placed,
        out_specs=(
            P("section", "ctx", None),
            P("section", "ctx", None),
            P("section", "ctx", None),
            P("section", "ctx", None),
        ),
        check_vma=False,
    )
```

```python
import math

import jax
import jax.numpy as jnp
from jax import lax
from jax.experimental import pallas as pl
from jax.experimental.pallas import tpu as pltpu
from jax.sharding import PartitionSpec as P


HEADS = 16
BLK = 128
SLOTS = 4


def passed_along(value, axis, steps):
    count = lax.axis_size(axis)
    pairs = [(source, (source + steps) % count) for source in range(count)]
    return lax.ppermute(value, axis, pairs)


def key_rows_of(qkv_ref, blocks, which):
    return jnp.concatenate([qkv_ref[b, which] for b in blocks], axis=0)


def forward_kernel(lay_ref, seg_ref, qkv_ref, o_ref, w_ref):
    block_count = qkv_ref.shape[0]
    head_dim = qkv_ref.shape[-1]
    score_scale = 1.0 / math.sqrt(head_dim)
    row = lax.broadcasted_iota(jnp.int32, (BLK, BLK), 0)
    col = lax.broadcasted_iota(jnp.int32, (BLK, BLK), 1)

    def body(a, carry):
        q = qkv_ref[a, 0]
        seg_a = seg_ref[a]
        blocks = [lay_ref[a * SLOTS + j] for j in range(SLOTS)]
        key_rows = key_rows_of(qkv_ref, blocks, 1)
        value_rows = key_rows_of(qkv_ref, blocks, 2)
        masks = []
        for b in blocks:
            diag = (b == a).astype(jnp.int32)
            open_ = jnp.logical_and(b < a, seg_ref[b] == seg_a).astype(jnp.int32)
            limit = row * diag + (1 - diag) * (open_ * BLK - 1)
            masks.append(col <= limit)
        visible = jnp.concatenate(masks, axis=1)
        scores = lax.dot_general(
            q, key_rows, (((1,), (1,)), ((), ())), preferred_element_type=jnp.float32
        ) * score_scale
        scores = jnp.where(visible, scores, -jnp.inf)
        row_max = jnp.max(scores, axis=-1, keepdims=True)
        raised = jnp.exp(scores - row_max)
        weights = raised / jnp.sum(raised, axis=-1, keepdims=True)
        w_ref[a] = weights
        o_ref[a] = jnp.dot(
            weights.astype(jnp.bfloat16), value_rows, preferred_element_type=jnp.float32
        ).astype(jnp.bfloat16)
        return carry

    lax.fori_loop(0, block_count, body, 0, unroll=4)


def backward_kernel(lay_ref, qkv_ref, g_ref, o_ref, w_ref, out_ref, dk_acc, dv_acc):
    block_count = qkv_ref.shape[0]
    head_dim = qkv_ref.shape[-1]
    score_scale = 1.0 / math.sqrt(head_dim)
    dk_acc[...] = jnp.zeros_like(dk_acc)
    dv_acc[...] = jnp.zeros_like(dv_acc)

    def body(a, carry):
        q = qkv_ref[a, 0]
        g = g_ref[a]
        blocks = [lay_ref[a * SLOTS + j] for j in range(SLOTS)]
        key_rows = key_rows_of(qkv_ref, blocks, 1)
        value_rows = key_rows_of(qkv_ref, blocks, 2)
        weights = w_ref[a]
        weights_low = weights.astype(jnp.bfloat16)
        grad_weight = lax.dot_general(
            g, value_rows, (((1,), (1,)), ((), ())), preferred_element_type=jnp.float32
        )
        row_inner = jnp.sum(
            g.astype(jnp.float32) * o_ref[a].astype(jnp.float32), axis=-1, keepdims=True
        )
        grad_score = (weights * (grad_weight - row_inner)).astype(jnp.bfloat16)
        grad_query = jnp.dot(grad_score, key_rows, preferred_element_type=jnp.float32)
        out_ref[a, 0] = (grad_query * score_scale).astype(jnp.bfloat16)
        grad_key_rows = lax.dot_general(
            grad_score, q, (((0,), (0,)), ((), ())), preferred_element_type=jnp.float32
        ) * score_scale
        grad_value_rows = lax.dot_general(
            weights_low, g, (((0,), (0,)), ((), ())), preferred_element_type=jnp.float32
        )
        for j, b in enumerate(blocks):
            dk_acc[b] += grad_key_rows[j * BLK:(j + 1) * BLK]
            dv_acc[b] += grad_value_rows[j * BLK:(j + 1) * BLK]
        return carry

    lax.fori_loop(0, block_count, body, 0, unroll=4)
    for b in range(block_count):
        out_ref[b, 1] = dk_acc[b].astype(jnp.bfloat16)
        out_ref[b, 2] = dv_acc[b].astype(jnp.bfloat16)


def forward_pass(plan, documents, qkv):
    block_count, _, rows, head_dim = qkv.shape
    flops = 2 * 2 * block_count * rows * SLOTS * rows * head_dim
    return pl.pallas_call(
        forward_kernel,
        out_shape=[
            jax.ShapeDtypeStruct((block_count, rows, head_dim), jnp.bfloat16),
            jax.ShapeDtypeStruct((block_count, rows, SLOTS * rows), jnp.float32),
        ],
        in_specs=[
            pl.BlockSpec(memory_space=pltpu.SMEM),
            pl.BlockSpec(memory_space=pltpu.SMEM),
            pl.BlockSpec(memory_space=pltpu.VMEM),
        ],
        out_specs=[pl.BlockSpec(memory_space=pltpu.VMEM)] * 2,
        cost_estimate=pl.CostEstimate(
            flops=flops,
            transcendentals=block_count * rows * SLOTS * rows,
            bytes_accessed=2 * 4 * block_count * rows * head_dim
            + 4 * block_count * rows * SLOTS * rows,
        ),
    )(plan, documents, qkv)


def backward_pass(plan, qkv, grad, attended, weights):
    block_count, _, rows, head_dim = qkv.shape
    flops = 4 * 2 * block_count * rows * SLOTS * rows * head_dim
    return pl.pallas_call(
        backward_kernel,
        out_shape=jax.ShapeDtypeStruct((block_count, 3, rows, head_dim), jnp.bfloat16),
        in_specs=[pl.BlockSpec(memory_space=pltpu.SMEM)]
        + [pl.BlockSpec(memory_space=pltpu.VMEM)] * 4,
        out_specs=pl.BlockSpec(memory_space=pltpu.VMEM),
        scratch_shapes=[
            pltpu.VMEM((block_count, rows, head_dim), jnp.float32),
            pltpu.VMEM((block_count, rows, head_dim), jnp.float32),
        ],
        cost_estimate=pl.CostEstimate(
            flops=flops,
            transcendentals=0,
            bytes_accessed=2 * 9 * block_count * rows * head_dim
            + 4 * block_count * rows * SLOTS * rows,
        ),
    )(plan, qkv, grad, attended, weights)


def shuffle_kernel(*refs):
    *in_refs, out_ref = refs
    head_count = out_ref.shape[0]
    head_dim = out_ref.shape[-1]
    for i, in_ref in enumerate(in_refs):
        for h in range(head_count):
            out_ref[h, i] = in_ref[0, :, h * head_dim:(h + 1) * head_dim]


def shuffle(fields, head_count):
    _, rows, width = fields[0].shape
    head_dim = width // head_count
    out = jax.ShapeDtypeStruct((head_count, len(fields), rows, head_dim), fields[0].dtype)
    return pl.pallas_call(
        shuffle_kernel,
        out_shape=out,
        in_specs=[pl.BlockSpec(memory_space=pltpu.VMEM)] * len(fields),
        out_specs=pl.BlockSpec(memory_space=pltpu.VMEM),
        cost_estimate=pl.CostEstimate(
            flops=0,
            transcendentals=0,
            bytes_accessed=4 * len(fields) * rows * width,
        ),
    )(*fields)


def unshuffle_kernel(first_ref, rest_ref, *out_refs):
    head_count, _, head_dim = first_ref.shape
    for i, out_ref in enumerate(out_refs):
        for h in range(head_count):
            piece = first_ref[h] if i == 0 else rest_ref[h, i - 1]
            out_ref[0, :, h * head_dim:(h + 1) * head_dim] = piece


def unshuffle(first, rest, section_rows):
    head_count, arrays, rows, head_dim = rest.shape
    field = jax.ShapeDtypeStruct((section_rows, rows, head_count * head_dim), rest.dtype)
    return pl.pallas_call(
        unshuffle_kernel,
        out_shape=[field] * (arrays + 1),
        in_specs=[pl.BlockSpec(memory_space=pltpu.VMEM)] * 2,
        out_specs=[pl.BlockSpec(memory_space=pltpu.VMEM)] * (arrays + 1),
        cost_estimate=pl.CostEstimate(
            flops=0,
            transcendentals=0,
            bytes_accessed=4 * (first.size + rest.size),
        ),
    )(first, rest)


def local(queries, key_states, value_states, upstream, layout, segments):
    section_rows, _, _ = queries.shape

    fields = shuffle((queries, key_states, value_states, upstream), HEADS)
    fields = lax.all_to_all(fields, "ctx", 0, 0, tiled=True)
    block_count = fields.shape[0]
    plan = layout[0, 0].reshape(block_count * SLOTS)
    documents = segments[0]
    grad = passed_along(fields[:, 3], "section", -1)
    attended, weights = forward_pass(plan, documents, fields)
    attended_back = lax.all_to_all(attended, "ctx", 0, 0, tiled=True)
    results = backward_pass(plan, fields, grad, attended, weights)
    back = lax.all_to_all(results, "ctx", 0, 0, tiled=True)
    return tuple(unshuffle(attended_back, back, section_rows))


def solution(mesh):
    placed = (
        P("section", "ctx", None),
        P("section", "ctx", None),
        P("section", "ctx", None),
        P("section", "ctx", None),
        P("section", "ctx", None, None),
        P("section", None),
    )
    return jax.shard_map(
        local,
        mesh=mesh,
        in_specs=placed,
        out_specs=(
            P("section", "ctx", None),
            P("section", "ctx", None),
            P("section", "ctx", None),
            P("section", "ctx", None),
        ),
        check_vma=False,
    )
```

```python
import math

import jax
import jax.numpy as jnp
from jax import lax
from jax.experimental import pallas as pl
from jax.experimental.pallas import tpu as pltpu
from jax.sharding import PartitionSpec as P


HEADS = 16
BLK = 128
SLOTS = 4


def passed_along(value, axis, steps):
    count = lax.axis_size(axis)
    pairs = [(source, (source + steps) % count) for source in range(count)]
    return lax.ppermute(value, axis, pairs)


def key_rows_of(qkv_ref, blocks, which):
    return jnp.concatenate([qkv_ref[b, which] for b in blocks], axis=0)


def forward_kernel(lay_ref, seg_ref, qkv_ref, o_ref, w_ref):
    block_count = qkv_ref.shape[0]
    head_dim = qkv_ref.shape[-1]
    score_scale = 1.0 / math.sqrt(head_dim)
    row = lax.broadcasted_iota(jnp.int32, (BLK, BLK), 0)
    col = lax.broadcasted_iota(jnp.int32, (BLK, BLK), 1)

    def body(a, carry):
        q = qkv_ref[a, 0]
        seg_a = seg_ref[a]
        blocks = [lay_ref[a * SLOTS + j] for j in range(SLOTS)]
        key_rows = key_rows_of(qkv_ref, blocks, 1)
        value_rows = key_rows_of(qkv_ref, blocks, 2)
        masks = []
        for b in blocks:
            diag = (b == a).astype(jnp.int32)
            open_ = jnp.logical_and(b < a, seg_ref[b] == seg_a).astype(jnp.int32)
            limit = row * diag + (1 - diag) * (open_ * BLK - 1)
            masks.append(col <= limit)
        visible = jnp.concatenate(masks, axis=1)
        scores = lax.dot_general(
            q, key_rows, (((1,), (1,)), ((), ())), preferred_element_type=jnp.float32
        ) * score_scale
        scores = jnp.where(visible, scores, -jnp.inf)
        row_max = jnp.max(scores, axis=-1, keepdims=True)
        raised = jnp.exp(scores - row_max)
        weights = raised / jnp.sum(raised, axis=-1, keepdims=True)
        w_ref[a] = weights
        o_ref[a] = jnp.dot(
            weights.astype(jnp.bfloat16), value_rows, preferred_element_type=jnp.float32
        ).astype(jnp.bfloat16)
        return carry

    lax.fori_loop(0, block_count, body, 0, unroll=4)


def backward_kernel(lay_ref, qkv_ref, g_ref, o_ref, w_ref, out_ref, dk_acc, dv_acc):
    block_count = qkv_ref.shape[0]
    head_dim = qkv_ref.shape[-1]
    score_scale = 1.0 / math.sqrt(head_dim)
    dk_acc[...] = jnp.zeros_like(dk_acc)
    dv_acc[...] = jnp.zeros_like(dv_acc)

    def body(a, carry):
        q = qkv_ref[a, 0]
        g = g_ref[a]
        blocks = [lay_ref[a * SLOTS + j] for j in range(SLOTS)]
        key_rows = key_rows_of(qkv_ref, blocks, 1)
        value_rows = key_rows_of(qkv_ref, blocks, 2)
        weights = w_ref[a]
        weights_low = weights.astype(jnp.bfloat16)
        grad_weight = lax.dot_general(
            g, value_rows, (((1,), (1,)), ((), ())), preferred_element_type=jnp.float32
        )
        row_inner = jnp.sum(
            g.astype(jnp.float32) * o_ref[a].astype(jnp.float32), axis=-1, keepdims=True
        )
        grad_score = (weights * (grad_weight - row_inner)).astype(jnp.bfloat16)
        grad_query = jnp.dot(grad_score, key_rows, preferred_element_type=jnp.float32)
        out_ref[a, 0] = (grad_query * score_scale).astype(jnp.bfloat16)
        grad_key_rows = lax.dot_general(
            grad_score, q, (((0,), (0,)), ((), ())), preferred_element_type=jnp.float32
        ) * score_scale
        grad_value_rows = lax.dot_general(
            weights_low, g, (((0,), (0,)), ((), ())), preferred_element_type=jnp.float32
        )
        for j, b in enumerate(blocks):
            dk_acc[b] += grad_key_rows[j * BLK:(j + 1) * BLK]
            dv_acc[b] += grad_value_rows[j * BLK:(j + 1) * BLK]
        return carry

    lax.fori_loop(0, block_count, body, 0, unroll=4)
    for b in range(block_count):
        out_ref[b, 1] = dk_acc[b].astype(jnp.bfloat16)
        out_ref[b, 2] = dv_acc[b].astype(jnp.bfloat16)


def forward_pass(plan, documents, qkv):
    block_count, _, rows, head_dim = qkv.shape
    flops = 2 * 2 * block_count * rows * SLOTS * rows * head_dim
    return pl.pallas_call(
        forward_kernel,
        out_shape=[
            jax.ShapeDtypeStruct((block_count, rows, head_dim), jnp.bfloat16),
            jax.ShapeDtypeStruct((block_count, rows, SLOTS * rows), jnp.float32),
        ],
        in_specs=[
            pl.BlockSpec(memory_space=pltpu.SMEM),
            pl.BlockSpec(memory_space=pltpu.SMEM),
            pl.BlockSpec(memory_space=pltpu.VMEM),
        ],
        out_specs=[pl.BlockSpec(memory_space=pltpu.VMEM)] * 2,
        cost_estimate=pl.CostEstimate(
            flops=flops,
            transcendentals=block_count * rows * SLOTS * rows,
            bytes_accessed=2 * 4 * block_count * rows * head_dim
            + 4 * block_count * rows * SLOTS * rows,
        ),
    )(plan, documents, qkv)


def backward_pass(plan, qkv, grad, attended, weights):
    block_count, _, rows, head_dim = qkv.shape
    flops = 4 * 2 * block_count * rows * SLOTS * rows * head_dim
    return pl.pallas_call(
        backward_kernel,
        out_shape=jax.ShapeDtypeStruct((block_count, 3, rows, head_dim), jnp.bfloat16),
        in_specs=[pl.BlockSpec(memory_space=pltpu.SMEM)]
        + [pl.BlockSpec(memory_space=pltpu.VMEM)] * 4,
        out_specs=pl.BlockSpec(memory_space=pltpu.VMEM),
        scratch_shapes=[
            pltpu.VMEM((block_count, rows, head_dim), jnp.float32),
            pltpu.VMEM((block_count, rows, head_dim), jnp.float32),
        ],
        cost_estimate=pl.CostEstimate(
            flops=flops,
            transcendentals=0,
            bytes_accessed=2 * 9 * block_count * rows * head_dim
            + 4 * block_count * rows * SLOTS * rows,
        ),
    )(plan, qkv, grad, attended, weights)


def shuffle_kernel(*refs):
    *in_refs, out_ref = refs
    head_count = out_ref.shape[0]
    head_dim = out_ref.shape[-1]
    for i, in_ref in enumerate(in_refs):
        for h in range(head_count):
            out_ref[h, i] = in_ref[0, :, h * head_dim:(h + 1) * head_dim]


def shuffle(fields, head_count):
    _, rows, width = fields[0].shape
    head_dim = width // head_count
    out = jax.ShapeDtypeStruct((head_count, len(fields), rows, head_dim), fields[0].dtype)
    return pl.pallas_call(
        shuffle_kernel,
        out_shape=out,
        in_specs=[pl.BlockSpec(memory_space=pltpu.VMEM)] * len(fields),
        out_specs=pl.BlockSpec(memory_space=pltpu.VMEM),
        cost_estimate=pl.CostEstimate(
            flops=0,
            transcendentals=0,
            bytes_accessed=4 * len(fields) * rows * width,
        ),
    )(*fields)


def unshuffle_kernel(first_ref, rest_ref, *out_refs):
    head_count, _, head_dim = first_ref.shape
    for i, out_ref in enumerate(out_refs):
        for h in range(head_count):
            piece = first_ref[h] if i == 0 else rest_ref[h, i - 1]
            out_ref[0, :, h * head_dim:(h + 1) * head_dim] = piece


def unshuffle(first, rest, section_rows):
    head_count, arrays, rows, head_dim = rest.shape
    field = jax.ShapeDtypeStruct((section_rows, rows, head_count * head_dim), rest.dtype)
    return pl.pallas_call(
        unshuffle_kernel,
        out_shape=[field] * (arrays + 1),
        in_specs=[pl.BlockSpec(memory_space=pltpu.VMEM)] * 2,
        out_specs=[pl.BlockSpec(memory_space=pltpu.VMEM)] * (arrays + 1),
        cost_estimate=pl.CostEstimate(
            flops=0,
            transcendentals=0,
            bytes_accessed=4 * (first.size + rest.size),
        ),
    )(first, rest)


def local(queries, key_states, value_states, upstream, layout, segments):
    section_rows = queries.shape[0]
    fields = shuffle((queries, key_states, value_states), HEADS)
    fields = lax.all_to_all(fields, "ctx", 0, 0, tiled=True)
    arrived = passed_along(upstream, "section", -1)
    grad = shuffle((arrived,), HEADS)
    grad = lax.all_to_all(grad, "ctx", 0, 0, tiled=True)[:, 0]
    block_count = fields.shape[0]
    plan = layout[0, 0].reshape(block_count * SLOTS)
    documents = segments[0]
    attended, weights = forward_pass(plan, documents, fields)
    attended_back = lax.all_to_all(attended, "ctx", 0, 0, tiled=True)
    results = backward_pass(plan, fields, grad, attended, weights)
    back = lax.all_to_all(results, "ctx", 0, 0, tiled=True)
    return tuple(unshuffle(attended_back, back, section_rows))


def solution(mesh):
    placed = (
        P("section", "ctx", None),
        P("section", "ctx", None),
        P("section", "ctx", None),
        P("section", "ctx", None),
        P("section", "ctx", None, None),
        P("section", None),
    )
    return jax.shard_map(
        local,
        mesh=mesh,
        in_specs=placed,
        out_specs=(
            P("section", "ctx", None),
            P("section", "ctx", None),
            P("section", "ctx", None),
            P("section", "ctx", None),
        ),
        check_vma=False,
    )
```

```python
import math

import jax
import jax.numpy as jnp
from jax import lax
from jax.experimental import pallas as pl
from jax.experimental.pallas import tpu as pltpu
from jax.sharding import PartitionSpec as P


HEADS = 16
BLK = 128
SLOTS = 4


def passed_along(value, axis, steps):
    count = lax.axis_size(axis)
    pairs = [(source, (source + steps) % count) for source in range(count)]
    return lax.ppermute(value, axis, pairs)


def key_rows_of(qkv_ref, blocks, which):
    return jnp.concatenate([qkv_ref[b, which] for b in blocks], axis=0)


def forward_kernel(lay_ref, seg_ref, qkv_ref, o_ref, w_ref):
    block_count = qkv_ref.shape[0]
    head_dim = qkv_ref.shape[-1]
    score_scale = 1.0 / math.sqrt(head_dim)
    row = lax.broadcasted_iota(jnp.int32, (BLK, BLK), 0)
    col = lax.broadcasted_iota(jnp.int32, (BLK, BLK), 1)

    def body(a, carry):
        q = qkv_ref[a, 0]
        seg_a = seg_ref[a]
        blocks = [lay_ref[a * SLOTS + j] for j in range(SLOTS)]
        key_rows = key_rows_of(qkv_ref, blocks, 1)
        value_rows = key_rows_of(qkv_ref, blocks, 2)
        masks = []
        for b in blocks:
            diag = (b == a).astype(jnp.int32)
            open_ = jnp.logical_and(b < a, seg_ref[b] == seg_a).astype(jnp.int32)
            limit = row * diag + (1 - diag) * (open_ * BLK - 1)
            masks.append(col <= limit)
        visible = jnp.concatenate(masks, axis=1)
        scores = lax.dot_general(
            q, key_rows, (((1,), (1,)), ((), ())), preferred_element_type=jnp.float32
        ) * score_scale
        scores = jnp.where(visible, scores, -jnp.inf)
        row_max = jnp.max(scores, axis=-1, keepdims=True)
        raised = jnp.exp(scores - row_max)
        weights = raised / jnp.sum(raised, axis=-1, keepdims=True)
        w_ref[a] = weights
        o_ref[a] = jnp.dot(
            weights.astype(jnp.bfloat16), value_rows, preferred_element_type=jnp.float32
        ).astype(jnp.bfloat16)
        return carry

    lax.fori_loop(0, block_count, body, 0, unroll=4)


def backward_kernel(lay_ref, qkv_ref, g_ref, o_ref, w_ref, out_ref, dk_acc, dv_acc):
    block_count = qkv_ref.shape[0]
    head_dim = qkv_ref.shape[-1]
    score_scale = 1.0 / math.sqrt(head_dim)
    dk_acc[...] = jnp.zeros_like(dk_acc)
    dv_acc[...] = jnp.zeros_like(dv_acc)

    def body(a, carry):
        q = qkv_ref[a, 0]
        g = g_ref[a]
        blocks = [lay_ref[a * SLOTS + j] for j in range(SLOTS)]
        key_rows = key_rows_of(qkv_ref, blocks, 1)
        value_rows = key_rows_of(qkv_ref, blocks, 2)
        weights = w_ref[a]
        weights_low = weights.astype(jnp.bfloat16)
        grad_weight = lax.dot_general(
            g, value_rows, (((1,), (1,)), ((), ())), preferred_element_type=jnp.float32
        )
        row_inner = jnp.sum(
            g.astype(jnp.float32) * o_ref[a].astype(jnp.float32), axis=-1, keepdims=True
        )
        grad_score = (weights * (grad_weight - row_inner)).astype(jnp.bfloat16)
        grad_query = jnp.dot(grad_score, key_rows, preferred_element_type=jnp.float32)
        out_ref[a, 0] = (grad_query * score_scale).astype(jnp.bfloat16)
        grad_key_rows = lax.dot_general(
            grad_score, q, (((0,), (0,)), ((), ())), preferred_element_type=jnp.float32
        ) * score_scale
        grad_value_rows = lax.dot_general(
            weights_low, g, (((0,), (0,)), ((), ())), preferred_element_type=jnp.float32
        )
        for j, b in enumerate(blocks):
            dk_acc[b] += grad_key_rows[j * BLK:(j + 1) * BLK]
            dv_acc[b] += grad_value_rows[j * BLK:(j + 1) * BLK]
        return carry

    lax.fori_loop(0, block_count, body, 0, unroll=4)
    for b in range(block_count):
        out_ref[b, 1] = dk_acc[b].astype(jnp.bfloat16)
        out_ref[b, 2] = dv_acc[b].astype(jnp.bfloat16)


def forward_pass(plan, documents, qkv):
    block_count, _, rows, head_dim = qkv.shape
    flops = 2 * 2 * block_count * rows * SLOTS * rows * head_dim
    return pl.pallas_call(
        forward_kernel,
        out_shape=[
            jax.ShapeDtypeStruct((block_count, rows, head_dim), jnp.bfloat16),
            jax.ShapeDtypeStruct((block_count, rows, SLOTS * rows), jnp.float32),
        ],
        in_specs=[
            pl.BlockSpec(memory_space=pltpu.SMEM),
            pl.BlockSpec(memory_space=pltpu.SMEM),
            pl.BlockSpec(memory_space=pltpu.VMEM),
        ],
        out_specs=[pl.BlockSpec(memory_space=pltpu.VMEM)] * 2,
        cost_estimate=pl.CostEstimate(
            flops=flops,
            transcendentals=block_count * rows * SLOTS * rows,
            bytes_accessed=2 * 4 * block_count * rows * head_dim
            + 4 * block_count * rows * SLOTS * rows,
        ),
    )(plan, documents, qkv)


def backward_pass(plan, qkv, grad, attended, weights):
    block_count, _, rows, head_dim = qkv.shape
    flops = 4 * 2 * block_count * rows * SLOTS * rows * head_dim
    return pl.pallas_call(
        backward_kernel,
        out_shape=jax.ShapeDtypeStruct((block_count, 3, rows, head_dim), jnp.bfloat16),
        in_specs=[pl.BlockSpec(memory_space=pltpu.SMEM)]
        + [pl.BlockSpec(memory_space=pltpu.VMEM)] * 4,
        out_specs=pl.BlockSpec(memory_space=pltpu.VMEM),
        scratch_shapes=[
            pltpu.VMEM((block_count, rows, head_dim), jnp.float32),
            pltpu.VMEM((block_count, rows, head_dim), jnp.float32),
        ],
        cost_estimate=pl.CostEstimate(
            flops=flops,
            transcendentals=0,
            bytes_accessed=2 * 9 * block_count * rows * head_dim
            + 4 * block_count * rows * SLOTS * rows,
        ),
    )(plan, qkv, grad, attended, weights)


def shuffle_kernel(*refs):
    *in_refs, out_ref = refs
    head_count = out_ref.shape[0]
    head_dim = out_ref.shape[-1]
    for i, in_ref in enumerate(in_refs):
        for h in range(head_count):
            out_ref[h, i] = in_ref[0, :, h * head_dim:(h + 1) * head_dim]


def shuffle(fields, head_count):
    _, rows, width = fields[0].shape
    head_dim = width // head_count
    out = jax.ShapeDtypeStruct((head_count, len(fields), rows, head_dim), fields[0].dtype)
    return pl.pallas_call(
        shuffle_kernel,
        out_shape=out,
        in_specs=[pl.BlockSpec(memory_space=pltpu.VMEM)] * len(fields),
        out_specs=pl.BlockSpec(memory_space=pltpu.VMEM),
        cost_estimate=pl.CostEstimate(
            flops=0,
            transcendentals=0,
            bytes_accessed=4 * len(fields) * rows * width,
        ),
    )(*fields)


def unshuffle_kernel(back_ref, *out_refs):
    head_count = back_ref.shape[0]
    head_dim = back_ref.shape[-1]
    for i, out_ref in enumerate(out_refs):
        for h in range(head_count):
            out_ref[0, :, h * head_dim:(h + 1) * head_dim] = back_ref[h, i]


def unshuffle(back, section_rows):
    head_count, arrays, rows, head_dim = back.shape
    field = jax.ShapeDtypeStruct((section_rows, rows, head_count * head_dim), back.dtype)
    return pl.pallas_call(
        unshuffle_kernel,
        out_shape=[field] * arrays,
        in_specs=[pl.BlockSpec(memory_space=pltpu.VMEM)],
        out_specs=[pl.BlockSpec(memory_space=pltpu.VMEM)] * arrays,
        cost_estimate=pl.CostEstimate(
            flops=0, transcendentals=0, bytes_accessed=4 * back.size
        ),
    )(back)


def local(queries, key_states, value_states, upstream, layout, segments):
    section_rows = queries.shape[0]
    fields = shuffle((queries, key_states, value_states), HEADS)
    fields = lax.all_to_all(fields, "ctx", 0, 0, tiled=True)
    arrived = passed_along(upstream, "section", -1)
    grad = shuffle((arrived,), HEADS)
    grad = lax.all_to_all(grad, "ctx", 0, 0, tiled=True)[:, 0]
    block_count = fields.shape[0]
    plan = layout[0, 0].reshape(block_count * SLOTS)
    documents = segments[0]
    attended, weights = forward_pass(plan, documents, fields)
    attended_back = lax.all_to_all(attended, "ctx", 0, 0, tiled=True)
    results = backward_pass(plan, fields, grad, attended, weights)
    back = lax.all_to_all(results, "ctx", 0, 0, tiled=True)
    (attended_out,) = unshuffle(attended_back[:, None], section_rows)
    return (attended_out, *unshuffle(back, section_rows))


def solution(mesh):
    placed = (
        P("section", "ctx", None),
        P("section", "ctx", None),
        P("section", "ctx", None),
        P("section", "ctx", None),
        P("section", "ctx", None, None),
        P("section", None),
    )
    return jax.shard_map(
        local,
        mesh=mesh,
        in_specs=placed,
        out_specs=(
            P("section", "ctx", None),
            P("section", "ctx", None),
            P("section", "ctx", None),
            P("section", "ctx", None),
        ),
        check_vma=False,
    )
```

```python
import math

import jax
import jax.numpy as jnp
from jax import lax
from jax.experimental import pallas as pl
from jax.experimental.pallas import tpu as pltpu
from jax.sharding import PartitionSpec as P


HEADS = 16
BLK = 128
SLOTS = 4


def passed_along(value, axis, steps):
    count = lax.axis_size(axis)
    pairs = [(source, (source + steps) % count) for source in range(count)]
    return lax.ppermute(value, axis, pairs)


def key_rows_of(qkv_ref, blocks, which):
    return jnp.concatenate([qkv_ref[b, which] for b in blocks], axis=0)


def forward_kernel(lay_ref, seg_ref, qkv_ref, o_ref, w_ref):
    block_count = qkv_ref.shape[0]
    head_dim = qkv_ref.shape[-1]
    score_scale = 1.0 / math.sqrt(head_dim)
    row = lax.broadcasted_iota(jnp.int32, (BLK, BLK), 0)
    col = lax.broadcasted_iota(jnp.int32, (BLK, BLK), 1)

    def body(a, carry):
        q = qkv_ref[a, 0]
        seg_a = seg_ref[a]
        blocks = [lay_ref[a * SLOTS + j] for j in range(SLOTS)]
        key_rows = key_rows_of(qkv_ref, blocks, 1)
        value_rows = key_rows_of(qkv_ref, blocks, 2)
        masks = []
        for b in blocks:
            diag = (b == a).astype(jnp.int32)
            open_ = jnp.logical_and(b < a, seg_ref[b] == seg_a).astype(jnp.int32)
            limit = row * diag + (1 - diag) * (open_ * BLK - 1)
            masks.append(col <= limit)
        visible = jnp.concatenate(masks, axis=1)
        scores = lax.dot_general(
            q, key_rows, (((1,), (1,)), ((), ())), preferred_element_type=jnp.float32
        ) * score_scale
        scores = jnp.where(visible, scores, -jnp.inf)
        row_max = jnp.max(scores, axis=-1, keepdims=True)
        raised = jnp.exp(scores - row_max)
        weights = raised / jnp.sum(raised, axis=-1, keepdims=True)
        w_ref[a] = weights
        o_ref[a] = jnp.dot(
            weights.astype(jnp.bfloat16), value_rows, preferred_element_type=jnp.float32
        ).astype(jnp.bfloat16)
        return carry

    lax.fori_loop(0, block_count, body, 0, unroll=4)


def backward_kernel(lay_ref, qkv_ref, g_ref, o_ref, w_ref, out_ref, dk_acc, dv_acc):
    block_count = qkv_ref.shape[0]
    head_dim = qkv_ref.shape[-1]
    score_scale = 1.0 / math.sqrt(head_dim)
    dk_acc[...] = jnp.zeros_like(dk_acc)
    dv_acc[...] = jnp.zeros_like(dv_acc)

    def body(a, carry):
        q = qkv_ref[a, 0]
        g = g_ref[a]
        blocks = [lay_ref[a * SLOTS + j] for j in range(SLOTS)]
        key_rows = key_rows_of(qkv_ref, blocks, 1)
        value_rows = key_rows_of(qkv_ref, blocks, 2)
        weights = w_ref[a]
        weights_low = weights.astype(jnp.bfloat16)
        grad_weight = lax.dot_general(
            g, value_rows, (((1,), (1,)), ((), ())), preferred_element_type=jnp.float32
        )
        row_inner = jnp.sum(
            g.astype(jnp.float32) * o_ref[a].astype(jnp.float32), axis=-1, keepdims=True
        )
        grad_score = (weights * (grad_weight - row_inner)).astype(jnp.bfloat16)
        grad_query = jnp.dot(grad_score, key_rows, preferred_element_type=jnp.float32)
        out_ref[a, 0] = o_ref[a]
        out_ref[a, 1] = (grad_query * score_scale).astype(jnp.bfloat16)
        grad_key_rows = lax.dot_general(
            grad_score, q, (((0,), (0,)), ((), ())), preferred_element_type=jnp.float32
        ) * score_scale
        grad_value_rows = lax.dot_general(
            weights_low, g, (((0,), (0,)), ((), ())), preferred_element_type=jnp.float32
        )
        for j, b in enumerate(blocks):
            dk_acc[b] += grad_key_rows[j * BLK:(j + 1) * BLK]
            dv_acc[b] += grad_value_rows[j * BLK:(j + 1) * BLK]
        return carry

    lax.fori_loop(0, block_count, body, 0, unroll=4)
    for b in range(block_count):
        out_ref[b, 2] = dk_acc[b].astype(jnp.bfloat16)
        out_ref[b, 3] = dv_acc[b].astype(jnp.bfloat16)


def forward_pass(plan, documents, qkv):
    block_count, _, rows, head_dim = qkv.shape
    flops = 2 * 2 * block_count * rows * SLOTS * rows * head_dim
    return pl.pallas_call(
        forward_kernel,
        out_shape=[
            jax.ShapeDtypeStruct((block_count, rows, head_dim), jnp.bfloat16),
            jax.ShapeDtypeStruct((block_count, rows, SLOTS * rows), jnp.float32),
        ],
        in_specs=[
            pl.BlockSpec(memory_space=pltpu.SMEM),
            pl.BlockSpec(memory_space=pltpu.SMEM),
            pl.BlockSpec(memory_space=pltpu.VMEM),
        ],
        out_specs=[pl.BlockSpec(memory_space=pltpu.VMEM)] * 2,
        cost_estimate=pl.CostEstimate(
            flops=flops,
            transcendentals=block_count * rows * SLOTS * rows,
            bytes_accessed=2 * 4 * block_count * rows * head_dim
            + 4 * block_count * rows * SLOTS * rows,
        ),
    )(plan, documents, qkv)


def backward_pass(plan, qkv, grad, attended, weights):
    block_count, _, rows, head_dim = qkv.shape
    flops = 4 * 2 * block_count * rows * SLOTS * rows * head_dim
    return pl.pallas_call(
        backward_kernel,
        out_shape=jax.ShapeDtypeStruct((block_count, 4, rows, head_dim), jnp.bfloat16),
        in_specs=[pl.BlockSpec(memory_space=pltpu.SMEM)]
        + [pl.BlockSpec(memory_space=pltpu.VMEM)] * 4,
        out_specs=pl.BlockSpec(memory_space=pltpu.VMEM),
        scratch_shapes=[
            pltpu.VMEM((block_count, rows, head_dim), jnp.float32),
            pltpu.VMEM((block_count, rows, head_dim), jnp.float32),
        ],
        cost_estimate=pl.CostEstimate(
            flops=flops,
            transcendentals=0,
            bytes_accessed=2 * 9 * block_count * rows * head_dim
            + 4 * block_count * rows * SLOTS * rows,
        ),
    )(plan, qkv, grad, attended, weights)


def shuffle_kernel(*refs):
    *in_refs, out_ref = refs
    head_count = out_ref.shape[0]
    head_dim = out_ref.shape[-1]
    for i, in_ref in enumerate(in_refs):
        for h in range(head_count):
            out_ref[h, i] = in_ref[0, :, h * head_dim:(h + 1) * head_dim]


def shuffle(fields, head_count):
    _, rows, width = fields[0].shape
    head_dim = width // head_count
    out = jax.ShapeDtypeStruct((head_count, len(fields), rows, head_dim), fields[0].dtype)
    return pl.pallas_call(
        shuffle_kernel,
        out_shape=out,
        in_specs=[pl.BlockSpec(memory_space=pltpu.VMEM)] * len(fields),
        out_specs=pl.BlockSpec(memory_space=pltpu.VMEM),
        cost_estimate=pl.CostEstimate(
            flops=0,
            transcendentals=0,
            bytes_accessed=4 * len(fields) * rows * width,
        ),
    )(*fields)


def unshuffle_kernel(back_ref, *out_refs):
    head_count = back_ref.shape[0]
    head_dim = back_ref.shape[-1]
    for i, out_ref in enumerate(out_refs):
        for h in range(head_count):
            out_ref[0, :, h * head_dim:(h + 1) * head_dim] = back_ref[h, i]


def unshuffle(back, section_rows):
    head_count, arrays, rows, head_dim = back.shape
    field = jax.ShapeDtypeStruct((section_rows, rows, head_count * head_dim), back.dtype)
    return pl.pallas_call(
        unshuffle_kernel,
        out_shape=[field] * arrays,
        in_specs=[pl.BlockSpec(memory_space=pltpu.VMEM)],
        out_specs=[pl.BlockSpec(memory_space=pltpu.VMEM)] * arrays,
        cost_estimate=pl.CostEstimate(
            flops=0, transcendentals=0, bytes_accessed=4 * back.size
        ),
    )(back)


def local(queries, key_states, value_states, upstream, layout, segments):
    section_rows = queries.shape[0]
    fields = shuffle((queries, key_states, value_states), HEADS)
    fields = lax.all_to_all(fields, "ctx", 0, 0, tiled=True)
    arrived = passed_along(upstream, "section", -1)
    grad = shuffle((arrived,), HEADS)
    grad = lax.all_to_all(grad, "ctx", 0, 0, tiled=True)[:, 0]
    block_count = fields.shape[0]
    plan = layout[0, 0].reshape(block_count * SLOTS)
    documents = segments[0]
    attended, weights = forward_pass(plan, documents, fields)
    results = backward_pass(plan, fields, grad, attended, weights)
    back = lax.all_to_all(results, "ctx", 0, 0, tiled=True)
    return tuple(unshuffle(back, section_rows))


def solution(mesh):
    placed = (
        P("section", "ctx", None),
        P("section", "ctx", None),
        P("section", "ctx", None),
        P("section", "ctx", None),
        P("section", "ctx", None, None),
        P("section", None),
    )
    return jax.shard_map(
        local,
        mesh=mesh,
        in_specs=placed,
        out_specs=(
            P("section", "ctx", None),
            P("section", "ctx", None),
            P("section", "ctx", None),
            P("section", "ctx", None),
        ),
        check_vma=False,
    )
```

```python
import math

import jax
import jax.numpy as jnp
from jax import lax
from jax.experimental import pallas as pl
from jax.experimental.pallas import tpu as pltpu
from jax.sharding import PartitionSpec as P


HEADS = 16
BLK = 128
SLOTS = 4


def passed_along(value, axis, steps):
    count = lax.axis_size(axis)
    pairs = [(source, (source + steps) % count) for source in range(count)]
    return lax.ppermute(value, axis, pairs)


def key_rows_of(qkv_ref, blocks, which):
    return jnp.concatenate([qkv_ref[b, which] for b in blocks], axis=0)


def forward_kernel(lay_ref, seg_ref, qkv_ref, o_ref, w_ref):
    block_count = qkv_ref.shape[0]
    head_dim = qkv_ref.shape[-1]
    score_scale = 1.0 / math.sqrt(head_dim)
    row = lax.broadcasted_iota(jnp.int32, (BLK, BLK), 0)
    col = lax.broadcasted_iota(jnp.int32, (BLK, BLK), 1)

    def body(a, carry):
        q = qkv_ref[a, 0]
        seg_a = seg_ref[a]
        blocks = [lay_ref[a * SLOTS + j] for j in range(SLOTS)]
        key_rows = key_rows_of(qkv_ref, blocks, 1)
        value_rows = key_rows_of(qkv_ref, blocks, 2)
        masks = []
        for b in blocks:
            diag = (b == a).astype(jnp.int32)
            open_ = jnp.logical_and(b < a, seg_ref[b] == seg_a).astype(jnp.int32)
            limit = row * diag + (1 - diag) * (open_ * BLK - 1)
            masks.append(col <= limit)
        visible = jnp.concatenate(masks, axis=1)
        scores = lax.dot_general(
            q, key_rows, (((1,), (1,)), ((), ())), preferred_element_type=jnp.float32
        ) * score_scale
        scores = jnp.where(visible, scores, -jnp.inf)
        row_max = jnp.max(scores, axis=-1, keepdims=True)
        raised = jnp.exp(scores - row_max)
        weights = raised / jnp.sum(raised, axis=-1, keepdims=True)
        w_ref[a] = weights
        o_ref[a] = jnp.dot(
            weights.astype(jnp.bfloat16), value_rows, preferred_element_type=jnp.float32
        ).astype(jnp.bfloat16)
        return carry

    lax.fori_loop(0, block_count, body, 0, unroll=4)


def backward_kernel(lay_ref, qkv_ref, g_ref, o_ref, w_ref, out_ref, dk_acc, dv_acc):
    block_count = qkv_ref.shape[0]
    head_dim = qkv_ref.shape[-1]
    score_scale = 1.0 / math.sqrt(head_dim)
    dk_acc[...] = jnp.zeros_like(dk_acc)
    dv_acc[...] = jnp.zeros_like(dv_acc)

    def body(a, carry):
        q = qkv_ref[a, 0]
        g = g_ref[a]
        blocks = [lay_ref[a * SLOTS + j] for j in range(SLOTS)]
        key_rows = key_rows_of(qkv_ref, blocks, 1)
        value_rows = key_rows_of(qkv_ref, blocks, 2)
        weights = w_ref[a]
        weights_low = weights.astype(jnp.bfloat16)
        grad_weight = lax.dot_general(
            g, value_rows, (((1,), (1,)), ((), ())), preferred_element_type=jnp.float32
        )
        row_inner = jnp.sum(
            g.astype(jnp.float32) * o_ref[a].astype(jnp.float32), axis=-1, keepdims=True
        )
        grad_score = (weights * (grad_weight - row_inner)).astype(jnp.bfloat16)
        grad_query = jnp.dot(grad_score, key_rows, preferred_element_type=jnp.float32)
        out_ref[a, 0] = (grad_query * score_scale).astype(jnp.bfloat16)
        grad_key_rows = lax.dot_general(
            grad_score, q, (((0,), (0,)), ((), ())), preferred_element_type=jnp.float32
        ) * score_scale
        grad_value_rows = lax.dot_general(
            weights_low, g, (((0,), (0,)), ((), ())), preferred_element_type=jnp.float32
        )
        for j, b in enumerate(blocks):
            dk_acc[b] += grad_key_rows[j * BLK:(j + 1) * BLK]
            dv_acc[b] += grad_value_rows[j * BLK:(j + 1) * BLK]
        return carry

    lax.fori_loop(0, block_count, body, 0, unroll=4)
    for b in range(block_count):
        out_ref[b, 1] = dk_acc[b].astype(jnp.bfloat16)
        out_ref[b, 2] = dv_acc[b].astype(jnp.bfloat16)


def forward_pass(plan, documents, qkv):
    block_count, _, rows, head_dim = qkv.shape
    flops = 2 * 2 * block_count * rows * SLOTS * rows * head_dim
    return pl.pallas_call(
        forward_kernel,
        out_shape=[
            jax.ShapeDtypeStruct((block_count, rows, head_dim), jnp.bfloat16),
            jax.ShapeDtypeStruct((block_count, rows, SLOTS * rows), jnp.float32),
        ],
        in_specs=[
            pl.BlockSpec(memory_space=pltpu.SMEM),
            pl.BlockSpec(memory_space=pltpu.SMEM),
            pl.BlockSpec(memory_space=pltpu.VMEM),
        ],
        out_specs=[pl.BlockSpec(memory_space=pltpu.VMEM)] * 2,
        cost_estimate=pl.CostEstimate(
            flops=flops,
            transcendentals=block_count * rows * SLOTS * rows,
            bytes_accessed=2 * 4 * block_count * rows * head_dim
            + 4 * block_count * rows * SLOTS * rows,
        ),
    )(plan, documents, qkv)


def backward_pass(plan, qkv, grad, attended, weights):
    block_count, _, rows, head_dim = qkv.shape
    flops = 4 * 2 * block_count * rows * SLOTS * rows * head_dim
    return pl.pallas_call(
        backward_kernel,
        out_shape=jax.ShapeDtypeStruct((block_count, 3, rows, head_dim), jnp.bfloat16),
        in_specs=[pl.BlockSpec(memory_space=pltpu.SMEM)]
        + [pl.BlockSpec(memory_space=pltpu.VMEM)] * 4,
        out_specs=pl.BlockSpec(memory_space=pltpu.VMEM),
        scratch_shapes=[
            pltpu.VMEM((block_count, rows, head_dim), jnp.float32),
            pltpu.VMEM((block_count, rows, head_dim), jnp.float32),
        ],
        cost_estimate=pl.CostEstimate(
            flops=flops,
            transcendentals=0,
            bytes_accessed=2 * 9 * block_count * rows * head_dim
            + 4 * block_count * rows * SLOTS * rows,
        ),
    )(plan, qkv, grad, attended, weights)


def shuffle_kernel(*refs):
    *in_refs, out_ref = refs
    for i, in_ref in enumerate(in_refs):
        out_ref[0, i] = in_ref[0]


def shuffle(fields, head_count):
    _, rows, width = fields[0].shape
    head_dim = width // head_count
    out = jax.ShapeDtypeStruct((head_count, len(fields), rows, head_dim), fields[0].dtype)
    return pl.pallas_call(
        shuffle_kernel,
        out_shape=out,
        grid=(head_count,),
        in_specs=[pl.BlockSpec((1, rows, head_dim), lambda h: (0, 0, h))] * len(fields),
        out_specs=pl.BlockSpec((1, len(fields), rows, head_dim), lambda h: (h, 0, 0, 0)),
        cost_estimate=pl.CostEstimate(
            flops=0,
            transcendentals=0,
            bytes_accessed=4 * len(fields) * rows * width,
        ),
    )(*fields)


def unshuffle_kernel(back_ref, *out_refs):
    for i, out_ref in enumerate(out_refs):
        out_ref[0] = back_ref[0, i]


def unshuffle(back, section_rows):
    head_count, arrays, rows, head_dim = back.shape
    field = jax.ShapeDtypeStruct((section_rows, rows, head_count * head_dim), back.dtype)
    return pl.pallas_call(
        unshuffle_kernel,
        out_shape=[field] * arrays,
        grid=(head_count,),
        in_specs=[pl.BlockSpec((1, arrays, rows, head_dim), lambda h: (h, 0, 0, 0))],
        out_specs=[pl.BlockSpec((1, rows, head_dim), lambda h: (0, 0, h))] * arrays,
        cost_estimate=pl.CostEstimate(
            flops=0, transcendentals=0, bytes_accessed=4 * back.size
        ),
    )(back)


def local(queries, key_states, value_states, upstream, layout, segments):
    section_rows = queries.shape[0]
    fields = shuffle((queries, key_states, value_states), HEADS)
    fields = lax.all_to_all(fields, "ctx", 0, 0, tiled=True)
    arrived = passed_along(upstream, "section", -1)
    grad = shuffle((arrived,), HEADS)
    grad = lax.all_to_all(grad, "ctx", 0, 0, tiled=True)[:, 0]
    block_count = fields.shape[0]
    plan = layout[0, 0].reshape(block_count * SLOTS)
    documents = segments[0]
    attended, weights = forward_pass(plan, documents, fields)
    attended_back = lax.all_to_all(attended, "ctx", 0, 0, tiled=True)
    results = backward_pass(plan, fields, grad, attended, weights)
    back = lax.all_to_all(results, "ctx", 0, 0, tiled=True)
    (attended_out,) = unshuffle(attended_back[:, None], section_rows)
    return (attended_out, *unshuffle(back, section_rows))


def solution(mesh):
    placed = (
        P("section", "ctx", None),
        P("section", "ctx", None),
        P("section", "ctx", None),
        P("section", "ctx", None),
        P("section", "ctx", None, None),
        P("section", None),
    )
    return jax.shard_map(
        local,
        mesh=mesh,
        in_specs=placed,
        out_specs=(
            P("section", "ctx", None),
            P("section", "ctx", None),
            P("section", "ctx", None),
            P("section", "ctx", None),
        ),
        check_vma=False,
    )
```

```python
import math

import jax
import jax.numpy as jnp
from jax import lax
from jax.experimental import pallas as pl
from jax.experimental.pallas import tpu as pltpu
from jax.sharding import PartitionSpec as P


HEADS = 16
BLK = 128
SLOTS = 4
GROUP = 4


def passed_along(value, axis, steps):
    count = lax.axis_size(axis)
    pairs = [(source, (source + steps) % count) for source in range(count)]
    return lax.ppermute(value, axis, pairs)


def key_rows_of(qkv_ref, blocks, which):
    return jnp.concatenate([qkv_ref[b, which] for b in blocks], axis=0)


def forward_kernel(lay_ref, seg_ref, qkv_ref, o_ref, w_ref):
    block_count = qkv_ref.shape[0]
    head_dim = qkv_ref.shape[-1]
    score_scale = 1.0 / math.sqrt(head_dim)
    row = lax.broadcasted_iota(jnp.int32, (BLK, BLK), 0)
    col = lax.broadcasted_iota(jnp.int32, (BLK, BLK), 1)

    def body(a, carry):
        q = qkv_ref[a, 0]
        seg_a = seg_ref[a]
        blocks = [lay_ref[a * SLOTS + j] for j in range(SLOTS)]
        key_rows = key_rows_of(qkv_ref, blocks, 1)
        value_rows = key_rows_of(qkv_ref, blocks, 2)
        masks = []
        for b in blocks:
            diag = (b == a).astype(jnp.int32)
            open_ = jnp.logical_and(b < a, seg_ref[b] == seg_a).astype(jnp.int32)
            limit = row * diag + (1 - diag) * (open_ * BLK - 1)
            masks.append(col <= limit)
        visible = jnp.concatenate(masks, axis=1)
        scores = lax.dot_general(
            q, key_rows, (((1,), (1,)), ((), ())), preferred_element_type=jnp.float32
        ) * score_scale
        scores = jnp.where(visible, scores, -jnp.inf)
        row_max = jnp.max(scores, axis=-1, keepdims=True)
        raised = jnp.exp(scores - row_max)
        weights = raised / jnp.sum(raised, axis=-1, keepdims=True)
        w_ref[a] = weights
        o_ref[a] = jnp.dot(
            weights.astype(jnp.bfloat16), value_rows, preferred_element_type=jnp.float32
        ).astype(jnp.bfloat16)
        return carry

    lax.fori_loop(0, block_count, body, 0, unroll=4)


def backward_kernel(lay_ref, qkv_ref, g_ref, o_ref, w_ref, out_ref, dk_acc, dv_acc):
    block_count = qkv_ref.shape[0]
    head_dim = qkv_ref.shape[-1]
    score_scale = 1.0 / math.sqrt(head_dim)
    dk_acc[...] = jnp.zeros_like(dk_acc)
    dv_acc[...] = jnp.zeros_like(dv_acc)

    def body(a, carry):
        q = qkv_ref[a, 0]
        g = g_ref[a]
        blocks = [lay_ref[a * SLOTS + j] for j in range(SLOTS)]
        key_rows = key_rows_of(qkv_ref, blocks, 1)
        value_rows = key_rows_of(qkv_ref, blocks, 2)
        weights = w_ref[a]
        weights_low = weights.astype(jnp.bfloat16)
        grad_weight = lax.dot_general(
            g, value_rows, (((1,), (1,)), ((), ())), preferred_element_type=jnp.float32
        )
        row_inner = jnp.sum(
            g.astype(jnp.float32) * o_ref[a].astype(jnp.float32), axis=-1, keepdims=True
        )
        grad_score = (weights * (grad_weight - row_inner)).astype(jnp.bfloat16)
        grad_query = jnp.dot(grad_score, key_rows, preferred_element_type=jnp.float32)
        out_ref[a, 0] = (grad_query * score_scale).astype(jnp.bfloat16)
        grad_key_rows = lax.dot_general(
            grad_score, q, (((0,), (0,)), ((), ())), preferred_element_type=jnp.float32
        ) * score_scale
        grad_value_rows = lax.dot_general(
            weights_low, g, (((0,), (0,)), ((), ())), preferred_element_type=jnp.float32
        )
        for j, b in enumerate(blocks):
            dk_acc[b] += grad_key_rows[j * BLK:(j + 1) * BLK]
            dv_acc[b] += grad_value_rows[j * BLK:(j + 1) * BLK]
        return carry

    lax.fori_loop(0, block_count, body, 0, unroll=4)
    for b in range(block_count):
        out_ref[b, 1] = dk_acc[b].astype(jnp.bfloat16)
        out_ref[b, 2] = dv_acc[b].astype(jnp.bfloat16)


def forward_pass(plan, documents, qkv):
    block_count, _, rows, head_dim = qkv.shape
    flops = 2 * 2 * block_count * rows * SLOTS * rows * head_dim
    return pl.pallas_call(
        forward_kernel,
        out_shape=[
            jax.ShapeDtypeStruct((block_count, rows, head_dim), jnp.bfloat16),
            jax.ShapeDtypeStruct((block_count, rows, SLOTS * rows), jnp.float32),
        ],
        in_specs=[
            pl.BlockSpec(memory_space=pltpu.SMEM),
            pl.BlockSpec(memory_space=pltpu.SMEM),
            pl.BlockSpec(memory_space=pltpu.VMEM),
        ],
        out_specs=[pl.BlockSpec(memory_space=pltpu.VMEM)] * 2,
        cost_estimate=pl.CostEstimate(
            flops=flops,
            transcendentals=block_count * rows * SLOTS * rows,
            bytes_accessed=2 * 4 * block_count * rows * head_dim
            + 4 * block_count * rows * SLOTS * rows,
        ),
    )(plan, documents, qkv)


def backward_pass(plan, qkv, grad, attended, weights):
    block_count, _, rows, head_dim = qkv.shape
    flops = 4 * 2 * block_count * rows * SLOTS * rows * head_dim
    return pl.pallas_call(
        backward_kernel,
        out_shape=jax.ShapeDtypeStruct((block_count, 3, rows, head_dim), jnp.bfloat16),
        in_specs=[pl.BlockSpec(memory_space=pltpu.SMEM)]
        + [pl.BlockSpec(memory_space=pltpu.VMEM)] * 4,
        out_specs=pl.BlockSpec(memory_space=pltpu.VMEM),
        scratch_shapes=[
            pltpu.VMEM((block_count, rows, head_dim), jnp.float32),
            pltpu.VMEM((block_count, rows, head_dim), jnp.float32),
        ],
        cost_estimate=pl.CostEstimate(
            flops=flops,
            transcendentals=0,
            bytes_accessed=2 * 9 * block_count * rows * head_dim
            + 4 * block_count * rows * SLOTS * rows,
        ),
    )(plan, qkv, grad, attended, weights)


def shuffle_kernel(*refs):
    *in_refs, out_ref = refs
    group, _, _, head_dim = out_ref.shape
    for i, in_ref in enumerate(in_refs):
        for h in range(group):
            out_ref[h, i] = in_ref[0, :, h * head_dim:(h + 1) * head_dim]


def shuffle(fields, head_count):
    _, rows, width = fields[0].shape
    head_dim = width // head_count
    out = jax.ShapeDtypeStruct((head_count, len(fields), rows, head_dim), fields[0].dtype)
    return pl.pallas_call(
        shuffle_kernel,
        out_shape=out,
        grid=(head_count // GROUP,),
        in_specs=[pl.BlockSpec((1, rows, GROUP * head_dim), lambda h: (0, 0, h))]
        * len(fields),
        out_specs=pl.BlockSpec(
            (GROUP, len(fields), rows, head_dim), lambda h: (h, 0, 0, 0)
        ),
        cost_estimate=pl.CostEstimate(
            flops=0,
            transcendentals=0,
            bytes_accessed=4 * len(fields) * rows * width,
        ),
    )(*fields)


def unshuffle_kernel(back_ref, *out_refs):
    group, _, _, head_dim = back_ref.shape
    for i, out_ref in enumerate(out_refs):
        for h in range(group):
            out_ref[0, :, h * head_dim:(h + 1) * head_dim] = back_ref[h, i]


def unshuffle(back, section_rows):
    head_count, arrays, rows, head_dim = back.shape
    field = jax.ShapeDtypeStruct((section_rows, rows, head_count * head_dim), back.dtype)
    return pl.pallas_call(
        unshuffle_kernel,
        out_shape=[field] * arrays,
        grid=(head_count // GROUP,),
        in_specs=[pl.BlockSpec((GROUP, arrays, rows, head_dim), lambda h: (h, 0, 0, 0))],
        out_specs=[pl.BlockSpec((1, rows, GROUP * head_dim), lambda h: (0, 0, h))]
        * arrays,
        cost_estimate=pl.CostEstimate(
            flops=0, transcendentals=0, bytes_accessed=4 * back.size
        ),
    )(back)


def local(queries, key_states, value_states, upstream, layout, segments):
    section_rows = queries.shape[0]
    fields = shuffle((queries, key_states, value_states), HEADS)
    fields = lax.all_to_all(fields, "ctx", 0, 0, tiled=True)
    arrived = passed_along(upstream, "section", -1)
    grad = shuffle((arrived,), HEADS)
    grad = lax.all_to_all(grad, "ctx", 0, 0, tiled=True)[:, 0]
    block_count = fields.shape[0]
    plan = layout[0, 0].reshape(block_count * SLOTS)
    documents = segments[0]
    attended, weights = forward_pass(plan, documents, fields)
    attended_back = lax.all_to_all(attended, "ctx", 0, 0, tiled=True)
    results = backward_pass(plan, fields, grad, attended, weights)
    back = lax.all_to_all(results, "ctx", 0, 0, tiled=True)
    (attended_out,) = unshuffle(attended_back[:, None], section_rows)
    return (attended_out, *unshuffle(back, section_rows))


def solution(mesh):
    placed = (
        P("section", "ctx", None),
        P("section", "ctx", None),
        P("section", "ctx", None),
        P("section", "ctx", None),
        P("section", "ctx", None, None),
        P("section", None),
    )
    return jax.shard_map(
        local,
        mesh=mesh,
        in_specs=placed,
        out_specs=(
            P("section", "ctx", None),
            P("section", "ctx", None),
            P("section", "ctx", None),
            P("section", "ctx", None),
        ),
        check_vma=False,
    )
```

```python
import math

import jax
import jax.numpy as jnp
from jax import lax
from jax.experimental import pallas as pl
from jax.experimental.pallas import tpu as pltpu
from jax.sharding import PartitionSpec as P


HEADS = 16
BLK = 128
SLOTS = 4


def passed_along(value, axis, steps):
    count = lax.axis_size(axis)
    pairs = [(source, (source + steps) % count) for source in range(count)]
    return lax.ppermute(value, axis, pairs)


def key_rows_of(qkv_ref, blocks, which):
    return jnp.concatenate([qkv_ref[b, which] for b in blocks], axis=0)


def forward_kernel(lay_ref, seg_ref, qkv_ref, o_ref, w_ref):
    block_count = qkv_ref.shape[0]
    head_dim = qkv_ref.shape[-1]
    score_scale = 1.0 / math.sqrt(head_dim)
    row = lax.broadcasted_iota(jnp.int32, (BLK, BLK), 0)
    col = lax.broadcasted_iota(jnp.int32, (BLK, BLK), 1)

    def body(a, carry):
        q = qkv_ref[a, 0]
        seg_a = seg_ref[a]
        blocks = [lay_ref[a * SLOTS + j] for j in range(SLOTS)]
        key_rows = key_rows_of(qkv_ref, blocks, 1)
        value_rows = key_rows_of(qkv_ref, blocks, 2)
        masks = []
        for b in blocks:
            diag = (b == a).astype(jnp.int32)
            open_ = jnp.logical_and(b < a, seg_ref[b] == seg_a).astype(jnp.int32)
            limit = row * diag + (1 - diag) * (open_ * BLK - 1)
            masks.append(col <= limit)
        visible = jnp.concatenate(masks, axis=1)
        scores = lax.dot_general(
            q, key_rows, (((1,), (1,)), ((), ())), preferred_element_type=jnp.float32
        ) * score_scale
        scores = jnp.where(visible, scores, -jnp.inf)
        row_max = jnp.max(scores, axis=-1, keepdims=True)
        raised = jnp.exp(scores - row_max)
        weights = raised / jnp.sum(raised, axis=-1, keepdims=True)
        w_ref[a] = weights
        o_ref[a] = jnp.dot(
            weights.astype(jnp.bfloat16), value_rows, preferred_element_type=jnp.float32
        ).astype(jnp.bfloat16)
        return carry

    lax.fori_loop(0, block_count, body, 0, unroll=4)


def backward_kernel(lay_ref, qkv_ref, g_ref, o_ref, w_ref, out_ref, dk_acc, dv_acc):
    block_count = qkv_ref.shape[0]
    head_dim = qkv_ref.shape[-1]
    score_scale = 1.0 / math.sqrt(head_dim)
    dk_acc[...] = jnp.zeros_like(dk_acc)
    dv_acc[...] = jnp.zeros_like(dv_acc)

    def body(a, carry):
        q = qkv_ref[a, 0]
        g = g_ref[a]
        blocks = [lay_ref[a * SLOTS + j] for j in range(SLOTS)]
        key_rows = key_rows_of(qkv_ref, blocks, 1)
        value_rows = key_rows_of(qkv_ref, blocks, 2)
        weights = w_ref[a]
        weights_low = weights.astype(jnp.bfloat16)
        grad_weight = lax.dot_general(
            g, value_rows, (((1,), (1,)), ((), ())), preferred_element_type=jnp.float32
        )
        row_inner = jnp.sum(
            g.astype(jnp.float32) * o_ref[a].astype(jnp.float32), axis=-1, keepdims=True
        )
        grad_score = (weights * (grad_weight - row_inner)).astype(jnp.bfloat16)
        grad_query = jnp.dot(grad_score, key_rows, preferred_element_type=jnp.float32)
        out_ref[a, 0] = (grad_query * score_scale).astype(jnp.bfloat16)
        grad_key_rows = lax.dot_general(
            grad_score, q, (((0,), (0,)), ((), ())), preferred_element_type=jnp.float32
        ) * score_scale
        grad_value_rows = lax.dot_general(
            weights_low, g, (((0,), (0,)), ((), ())), preferred_element_type=jnp.float32
        )
        for j, b in enumerate(blocks):
            dk_acc[b] += grad_key_rows[j * BLK:(j + 1) * BLK]
            dv_acc[b] += grad_value_rows[j * BLK:(j + 1) * BLK]
        return carry

    lax.fori_loop(0, block_count, body, 0, unroll=4)
    for b in range(block_count):
        out_ref[b, 1] = dk_acc[b].astype(jnp.bfloat16)
        out_ref[b, 2] = dv_acc[b].astype(jnp.bfloat16)


def forward_pass(plan, documents, qkv):
    block_count, _, rows, head_dim = qkv.shape
    flops = 2 * 2 * block_count * rows * SLOTS * rows * head_dim
    return pl.pallas_call(
        forward_kernel,
        out_shape=[
            jax.ShapeDtypeStruct((block_count, rows, head_dim), jnp.bfloat16),
            jax.ShapeDtypeStruct((block_count, rows, SLOTS * rows), jnp.float32),
        ],
        in_specs=[
            pl.BlockSpec(memory_space=pltpu.SMEM),
            pl.BlockSpec(memory_space=pltpu.SMEM),
            pl.BlockSpec(memory_space=pltpu.VMEM),
        ],
        out_specs=[pl.BlockSpec(memory_space=pltpu.VMEM)] * 2,
        cost_estimate=pl.CostEstimate(
            flops=flops,
            transcendentals=block_count * rows * SLOTS * rows,
            bytes_accessed=2 * 4 * block_count * rows * head_dim
            + 4 * block_count * rows * SLOTS * rows,
        ),
    )(plan, documents, qkv)


def backward_pass(plan, qkv, grad, attended, weights):
    block_count, _, rows, head_dim = qkv.shape
    flops = 4 * 2 * block_count * rows * SLOTS * rows * head_dim
    return pl.pallas_call(
        backward_kernel,
        out_shape=jax.ShapeDtypeStruct((block_count, 3, rows, head_dim), jnp.bfloat16),
        in_specs=[pl.BlockSpec(memory_space=pltpu.SMEM)]
        + [pl.BlockSpec(memory_space=pltpu.VMEM)] * 4,
        out_specs=pl.BlockSpec(memory_space=pltpu.VMEM),
        scratch_shapes=[
            pltpu.VMEM((block_count, rows, head_dim), jnp.float32),
            pltpu.VMEM((block_count, rows, head_dim), jnp.float32),
        ],
        cost_estimate=pl.CostEstimate(
            flops=flops,
            transcendentals=0,
            bytes_accessed=2 * 9 * block_count * rows * head_dim
            + 4 * block_count * rows * SLOTS * rows,
        ),
    )(plan, qkv, grad, attended, weights)


def shuffle_kernel(*refs):
    *in_refs, out_ref = refs
    head_count = out_ref.shape[0]
    head_dim = out_ref.shape[-1]
    for i, in_ref in enumerate(in_refs):
        for h in range(head_count):
            out_ref[h, i] = in_ref[0, :, h * head_dim:(h + 1) * head_dim]


def shuffle(fields, head_count):
    _, rows, width = fields[0].shape
    head_dim = width // head_count
    out = jax.ShapeDtypeStruct((head_count, len(fields), rows, head_dim), fields[0].dtype)
    return pl.pallas_call(
        shuffle_kernel,
        out_shape=out,
        in_specs=[pl.BlockSpec(memory_space=pltpu.VMEM)] * len(fields),
        out_specs=pl.BlockSpec(memory_space=pltpu.VMEM),
        cost_estimate=pl.CostEstimate(
            flops=0,
            transcendentals=0,
            bytes_accessed=4 * len(fields) * rows * width,
        ),
    )(*fields)


def unshuffle_kernel(back_hbm, *refs):
    *out_refs, buf, sems = refs
    head_count = back_hbm.shape[0]
    head_dim = back_hbm.shape[-1]
    copies = [
        pltpu.make_async_copy(back_hbm.at[h], buf.at[h], sems.at[h])
        for h in range(head_count)
    ]
    for copy in copies:
        copy.start()
    for h, copy in enumerate(copies):
        copy.wait()
        for i, out_ref in enumerate(out_refs):
            out_ref[0, :, h * head_dim:(h + 1) * head_dim] = buf[h, i]


def unshuffle(back, section_rows):
    head_count, arrays, rows, head_dim = back.shape
    field = jax.ShapeDtypeStruct((section_rows, rows, head_count * head_dim), back.dtype)
    return pl.pallas_call(
        unshuffle_kernel,
        out_shape=[field] * arrays,
        in_specs=[pl.BlockSpec(memory_space=pl.ANY)],
        out_specs=[pl.BlockSpec(memory_space=pltpu.VMEM)] * arrays,
        scratch_shapes=[
            pltpu.VMEM(back.shape, back.dtype),
            pltpu.SemaphoreType.DMA((head_count,)),
        ],
        cost_estimate=pl.CostEstimate(
            flops=0, transcendentals=0, bytes_accessed=4 * back.size
        ),
    )(back)


def local(queries, key_states, value_states, upstream, layout, segments):
    section_rows = queries.shape[0]
    fields = shuffle((queries, key_states, value_states), HEADS)
    fields = lax.all_to_all(fields, "ctx", 0, 0, tiled=True)
    arrived = passed_along(upstream, "section", -1)
    grad = shuffle((arrived,), HEADS)
    grad = lax.all_to_all(grad, "ctx", 0, 0, tiled=True)[:, 0]
    block_count = fields.shape[0]
    plan = layout[0, 0].reshape(block_count * SLOTS)
    documents = segments[0]
    attended, weights = forward_pass(plan, documents, fields)
    attended_back = lax.all_to_all(attended, "ctx", 0, 0, tiled=True)
    results = backward_pass(plan, fields, grad, attended, weights)
    back = lax.all_to_all(results, "ctx", 0, 0, tiled=True)
    (attended_out,) = unshuffle(attended_back[:, None], section_rows)
    return (attended_out, *unshuffle(back, section_rows))


def solution(mesh):
    placed = (
        P("section", "ctx", None),
        P("section", "ctx", None),
        P("section", "ctx", None),
        P("section", "ctx", None),
        P("section", "ctx", None, None),
        P("section", None),
    )
    return jax.shard_map(
        local,
        mesh=mesh,
        in_specs=placed,
        out_specs=(
            P("section", "ctx", None),
            P("section", "ctx", None),
            P("section", "ctx", None),
            P("section", "ctx", None),
        ),
        check_vma=False,
    )
```
